256 devices in a mesh: sub: 64 (over z, x, core), harm: 4 (over y).
Axes of the slice: x: 4, y: 4, z: 8, core: 2. Of those that a mesh axis runs over, the one named last changes fastest.
Arguments:
- right_side: float32 [16, 128, 16384], P(None, None, 'sub'), may hold values from -6 to 6
- border_side: float32 [16, 128, 2048], P(None, None, 'sub'), may hold values from -6 to 6
- precond_tiles: bfloat16 [32768, 128, 128], P('sub', 'harm'), may hold values from -0.375 to 0.375
- tile_out: int32 [32768], P('sub'), may hold values from 0 to 255
- tile_in: int32 [32768], P('sub'), may hold values from 0 to 255
- couple_tiles: bfloat16 [16384, 128, 128], P('sub', 'harm'), may hold values from -0.1875 to 0.1875
- return_tiles: bfloat16 [16384, 128, 128], P('sub', 'harm'), may hold values from -0.5 to 0.5
- couple_node: int32 [16384], P('sub'), may hold values from 0 to 255
- border_owner: int32 [16384, 1], P('sub'), may hold values from 0 to 63; in each aligned block of 256 rows (0 to 255, 256 to 511, ...) at most 8 rows name the same one
- border_row: int32 [16384], P('sub'), may hold values from 0 to 31
- border_inverse: bfloat16 [2048, 128, 128], P('sub', 'harm'), may hold values from -0.5 to 0.5
Outputs:
- interior_update: float32 [16, 128, 16384], P(None, 'harm', 'sub')
- border_update: float32 [16, 128, 2048], P(None, 'harm', 'sub')
The draws below stay inside these ranges and needn't reach their ends.
Inputs may be any that keep to these rules, and one draw needn't show every extreme that they name: `border_owner`: among the rows of one subcircuit at most 8 name one owner, a bound that some block reaches of them.
All inputs are finite; a program needn't handle non-finite values.
Results may differ from the reference program's by a relative error of at most 0.005.
Values may be sent and summed in bfloat16 or wider, within the bound.
No kernel may reach another device: no remote copies, remote signals or barrier semaphores. Data moves between devices by JAX's collectives and lax.ppermute only.
A program may use at most 128 MiB of HBM per device.

```python
import math
import jax
import jax.numpy as jnp
import numpy as np
from jax import lax

H = 128
R = 16
NL = 256
NT = 512
BT = 256
BD = 32
CAP = 8
NODES = 16384
NBORD = 2048
NTI = 32768
NBT = 16384
N_SUB = 64


def touch_ends(array, rng, low, high):
    dims = array.shape
    index_at = [jax.random.randint(jax.random.fold_in(rng, axis), (), 0, dims[axis]) for axis in range(len(dims))]
    array = array.at[tuple(index_at)].set(low)
    longest = dims.index(max(dims))
    index_at[longest] = (index_at[longest] + 1) % dims[longest]
    return array.at[tuple(index_at)].set(high)


def block_levels(rng, dims, cuts, smallest, top_value):
    def one(position, blocks):
        heights = jax.random.uniform(jax.random.fold_in(jax.random.fold_in(rng, 6), position), (blocks,), jnp.float32, smallest / len(cuts), top_value / len(cuts))
        return jnp.repeat(jnp.exp(heights), dims[position] // blocks).reshape((-1,) + (1,) * (len(dims) - position - 1))

    gain = one(*cuts[0])
    for cut in cuts[1:]:
        gain = gain * one(*cut)
    return gain


def assign_block(key, own, number, rows, count, top, reach, slope):
    order = jax.random.permutation(key, count)
    packed, common = load_shares(count, rows * top, reach, slope, True), load_shares(count, rows * top, reach, slope, False)
    places = jnp.arange(count)

    def named(lengths, rotation):
        used = int((lengths > 0).sum())
        fixed = max(1, used // 4)
        shifted = fixed + (places - fixed + rotation * (used - fixed)) % max(1, count - fixed)
        return jnp.zeros((count,), jnp.int32).at[order[jnp.where(places < fixed, places, shifted)]].set(jnp.asarray(lengths, jnp.int32))

    lengths = jnp.where(number % 4 == 0, named(packed, number // 4), named(common, number - number // 4 - 1))
    mixed = jax.random.permutation(jax.random.fold_in(own, 3), count)
    giver, taker = mixed[0:count // 2 * 2:2], mixed[1:count // 2 * 2:2]
    margin = jnp.minimum(lengths[giver] - 1, reach - lengths[taker]) // 2
    margin = jnp.where((giver == order[0]) | (taker == order[0]) | (lengths[taker] == 0), 0, jnp.maximum(margin, 0))
    shifted = jax.random.randint(jax.random.fold_in(own, 4), (count // 2,), 0, 1 << 20) % (margin + 1)
    lengths = lengths.at[giver].add(-shifted).at[taker].add(shifted)
    labels = jnp.searchsorted(jnp.cumsum(lengths), jnp.arange(rows * top), side="right").astype(jnp.int32)
    table = labels.reshape(top, rows).T
    table = table[jax.random.permutation(jax.random.fold_in(own, 1), rows)]
    rotation = jax.random.randint(jax.random.fold_in(own, 2), (rows, 1), 0, top)
    return jnp.take_along_axis(table, (jnp.arange(top)[None, :] + rotation) % top, axis=1)


def load_shares(count, total, limit, skew, full):
    loads = [(1 << 20) // math.isqrt(standing ** skew) + 1 for standing in range(1, count + 1)]
    largest = limit if full else min(limit, max(-(-total // count), total * loads[0] // sum(loads)))
    least = 1 if total - largest >= count - 1 else 0
    counts, spare = [largest] + [least] * (count - 1), total - largest - least * (count - 1)
    while spare > 0:
        free = [i for i in range(1, count) if counts[i] < largest] or [i for i in range(1, count) if counts[i] < limit]
        whole, budget = sum([loads[i] for i in free]), spare
        for i in free:
            addition = min(limit - counts[i], max(1, budget * loads[i] // whole), spare)
            counts[i] = counts[i] + addition
            spare = spare - addition
    return np.array(counts)


def centred(stream_key, extent, spread, limit, cuts=(), held_as=jnp.bfloat16):
    result = spread * jax.random.normal(stream_key, extent, jnp.float32)
    if cuts:
        result = result * block_levels(stream_key, extent, cuts, -0.22, 0.18)
    return jnp.clip(result, -limit, limit).astype(held_as)


def setup_inputs(seed: int = 0) -> dict:
    arg_keys = jax.random.split(jax.random.key(seed), 12)
    right_side = centred(arg_keys[0], (R, H, NODES), 1.0, 6.0, ((2, 64),), jnp.float32)
    border_side = centred(arg_keys[1], (R, H, NBORD), 1.0, 6.0, ((2, 64),), jnp.float32)
    precond_tiles = centred(arg_keys[2], (NTI, H, H), (2 * H) ** -0.5, 0.375, ((0, 64), (1, 4)))
    tile_out = touch_ends(jax.random.randint(arg_keys[3], (NTI,), 0, NL), jax.random.fold_in(arg_keys[3], 1), 0, NL - 1).astype(jnp.int32)
    tile_in = touch_ends(jax.random.randint(arg_keys[4], (NTI,), 0, NL), jax.random.fold_in(arg_keys[4], 1), 0, NL - 1).astype(jnp.int32)
    couple_tiles = centred(arg_keys[5], (NBT, H, H), (8 * H) ** -0.5, 0.1875, ((0, 64), (1, 4)))
    return_tiles = centred(arg_keys[6], (NBT, H, H), H ** -0.5, 0.5, ((0, 64), (1, 4)))
    couple_node = touch_ends(jax.random.randint(arg_keys[7], (NBT,), 0, NL), jax.random.fold_in(arg_keys[7], 1), 0, NL - 1).astype(jnp.int32)
    border_owner_keys = jax.random.split(jax.random.fold_in(arg_keys[8], 1), NBT // BT)
    border_owner_turns = jax.random.permutation(jax.random.fold_in(arg_keys[8], 3), NBT // BT)
    border_owner = jax.vmap(lambda own, number: assign_block(jax.random.fold_in(arg_keys[8], 2), own, number, BT, N_SUB, 1, CAP, 2))(border_owner_keys, border_owner_turns).reshape((NBT, 1))
    border_row = touch_ends(jax.random.randint(arg_keys[9], (NBT,), 0, BD), jax.random.fold_in(arg_keys[9], 1), 0, BD - 1).astype(jnp.int32)
    border_inverse = centred(arg_keys[10], (NBORD, H, H), H ** -0.5, 0.5, ((0, 64), (1, 4)))
    return {"right_side": right_side, "border_side": border_side, "precond_tiles": precond_tiles, "tile_out": tile_out, "tile_in": tile_in, "couple_tiles": couple_tiles, "return_tiles": return_tiles, "couple_node": couple_node, "border_owner": border_owner, "border_row": border_row, "border_inverse": border_inverse}


def tile_product(tile_set, columns, targets, segment_total):
    product = jnp.einsum('tok,trk->tro', tile_set.astype(jnp.float32), columns.astype(jnp.float32))
    return jax.ops.segment_sum(product, targets, num_segments=segment_total)


def reference(right_side, border_side, precond_tiles, tile_out, tile_in, couple_tiles, return_tiles, couple_node, border_owner, border_row, border_inverse):
    side_nodes = jnp.transpose(right_side.reshape(R, H, N_SUB, NL), (2, 3, 0, 1))
    tiles_sub = precond_tiles.reshape(N_SUB, NT, H, H)
    out_sub = tile_out.reshape(N_SUB, NT)
    in_sub = tile_in.reshape(N_SUB, NT)
    couple_sub = couple_tiles.reshape(N_SUB, BT, H, H)
    return_sub = return_tiles.reshape(N_SUB, BT, H, H)
    node_sub = couple_node.reshape(N_SUB, BT)
    border_index = (border_owner[:, 0] * BD + border_row).astype(jnp.int32)
    index_sub = border_index.reshape(N_SUB, BT)

    def first_section(pieces):
        tile_set, out_list, in_list, side_block, couple_set, node_list = pieces
        side_low = side_block.astype(jnp.bfloat16)
        first_pass = tile_product(tile_set, side_low[in_list], out_list, NL).astype(jnp.bfloat16)
        return jnp.einsum('tok,trk->tro', couple_set.astype(jnp.float32), first_pass[node_list].astype(jnp.float32))

    partials = lax.map(first_section, (tiles_sub, out_sub, in_sub, side_nodes, couple_sub, node_sub))
    incoming = jax.ops.segment_sum(partials.reshape(N_SUB * BT, R, H), border_index, num_segments=N_SUB * BD)
    border_nodes = jnp.transpose(border_side, (2, 0, 1))
    residual_low = (border_nodes - incoming).astype(jnp.bfloat16)
    solved = jnp.einsum('bok,brk->bro', border_inverse.astype(jnp.float32), residual_low.astype(jnp.float32))
    solved_low = solved.astype(jnp.bfloat16)

    def second_section(pieces):
        tile_set, out_list, in_list, side_block, back_set, node_list, index_list = pieces
        correction = tile_product(back_set, solved_low[index_list], node_list, NL)
        update_low = (side_block - correction).astype(jnp.bfloat16)
        return tile_product(tile_set, update_low[in_list], out_list, NL)

    second_pass = lax.map(second_section, (tiles_sub, out_sub, in_sub, side_nodes, return_sub, node_sub, index_sub))
    interior = jnp.transpose(second_pass, (2, 3, 0, 1)).reshape(R, H, N_SUB * NL)
    return interior, jnp.transpose(solved, (1, 2, 0))
```

```python
import jax
import jax.numpy as jnp
from jax import lax
from jax.sharding import PartitionSpec as P


def collect(values, targets, row_total, first_row=0):
    marks = (
        first_row + jnp.arange(row_total, dtype=jnp.int32)[:, None] == targets[None, :]
    ).astype(jnp.float32)
    flat_rows = values.reshape(values.shape[0], -1)
    summed = jnp.dot(
        marks, flat_rows, precision=lax.Precision.HIGHEST, preferred_element_type=jnp.float32
    )
    return summed.reshape((row_total,) + values.shape[1:])


def tile_product(tile_set, columns, targets, segment_total):
    product = jnp.einsum("tok,trk->tro", tile_set, columns, preferred_element_type=jnp.float32)
    return collect(product, targets, segment_total)


def harm_gather(values, axis):
    count = lax.axis_size("harm")
    own = lax.axis_index("harm")
    parts = [values] + [
        lax.ppermute(values, "harm", [(i, (i + s) % count) for i in range(count)])
        for s in range(1, count)
    ]
    ahead = jnp.stack([parts[(-m) % count] for m in range(count)] * 2, 0)
    ordered = lax.dynamic_slice_in_dim(ahead, (count - own) % count, count, 0)
    ordered = jnp.moveaxis(ordered, 0, axis)
    shape = values.shape[:axis] + (count * values.shape[axis],) + values.shape[axis + 1 :]
    return ordered.reshape(shape)


def on_device(
    right_side,
    border_side,
    precond_tiles,
    tile_out,
    tile_in,
    couple_tiles,
    return_tiles,
    couple_node,
    border_owner,
    border_row,
    border_inverse,
):
    harm_block = precond_tiles.shape[1]
    node_count = right_side.shape[2]
    row_count = border_side.shape[2]
    touch_count = couple_node.shape[0]
    sub_count = lax.axis_size("sub")
    harm_offset = lax.axis_index("harm") * harm_block
    side_nodes = jnp.transpose(right_side, (2, 0, 1))
    border_nodes = jnp.transpose(border_side, (2, 0, 1))
    own_border = lax.dynamic_slice_in_dim(border_nodes, harm_offset, harm_block, 2)
    own_side = lax.dynamic_slice_in_dim(side_nodes, harm_offset, harm_block, 2)
    side_low = side_nodes.astype(jnp.bfloat16)
    first_pass = tile_product(precond_tiles, side_low[tile_in], tile_out, node_count).astype(
        jnp.bfloat16
    )
    first_full = harm_gather(first_pass, 2)
    partials = jnp.einsum(
        "tok,trk->tro", couple_tiles, first_full[couple_node], preferred_element_type=jnp.float32
    )
    owner_list = border_owner[:, 0]
    value_shape = partials.shape[1:]
    capacity = min(touch_count, max(4, 2 * touch_count // sub_count))
    owner_marks = (owner_list[:, None] == jnp.arange(sub_count, dtype=jnp.int32)[None, :]).astype(
        jnp.int32
    )
    earlier = jnp.cumsum(owner_marks, axis=0) - owner_marks
    slot_index = owner_list * capacity + jnp.sum(earlier * owner_marks, axis=1)
    slot_place = jnp.arange(sub_count * capacity, dtype=jnp.int32)[:, None] == slot_index[None, :]
    place_float = slot_place.astype(jnp.float32)
    send_values = jnp.dot(
        place_float,
        partials.reshape(touch_count, -1),
        precision=lax.Precision.HIGHEST,
        preferred_element_type=jnp.float32,
    )
    send_rows = jnp.sum(slot_place.astype(jnp.int32) * border_row[None, :], axis=1)
    send_values = send_values.reshape((sub_count, capacity) + value_shape)
    send_rows = send_rows.reshape((sub_count, capacity))
    arrived, arrived_rows = (
        lax.all_to_all(
            send_values.astype(jnp.bfloat16), "sub", split_axis=0, concat_axis=0, tiled=True
        ).astype(jnp.float32),
        lax.all_to_all(send_rows, "sub", split_axis=0, concat_axis=0, tiled=True),
    )
    incoming = collect(
        arrived.reshape((sub_count * capacity,) + value_shape), arrived_rows.reshape(-1), row_count
    )
    residual_low = (own_border - incoming).astype(jnp.bfloat16)
    residual_full = harm_gather(residual_low, 2)
    solved = jnp.einsum(
        "bok,brk->bro", border_inverse, residual_full, preferred_element_type=jnp.float32
    )
    solved, solved_low = (solved, solved.astype(jnp.bfloat16))
    replies = solved_low[arrived_rows]
    returned = lax.all_to_all(replies, "sub", split_axis=0, concat_axis=0, tiled=True)
    returned_flat = returned.reshape(sub_count * capacity, -1)
    touch_low = jnp.dot(
        slot_place.astype(jnp.bfloat16).T, returned_flat, preferred_element_type=jnp.float32
    )
    touch_low = touch_low.astype(jnp.bfloat16).reshape((touch_count,) + value_shape)
    touch_full = harm_gather(touch_low, 2)
    correction = tile_product(return_tiles, touch_full, couple_node, node_count)
    update_low = (own_side - correction).astype(jnp.bfloat16)
    update_full = harm_gather(update_low, 2)
    second_pass = tile_product(precond_tiles, update_full[tile_in], tile_out, node_count)
    return (jnp.transpose(second_pass, (1, 2, 0)), jnp.transpose(solved, (1, 2, 0)))


def solution(mesh):
    in_specs = (
        P(None, None, "sub"),
        P(None, None, "sub"),
        P("sub", "harm", None),
        P("sub"),
        P("sub"),
        P("sub", "harm", None),
        P("sub", "harm", None),
        P("sub"),
        P("sub", None),
        P("sub"),
        P("sub", "harm", None),
    )
    out_specs = (P(None, "harm", "sub"), P(None, "harm", "sub"))
    return jax.shard_map(
        on_device, mesh=mesh, in_specs=in_specs, out_specs=out_specs, check_vma=False
    )
```

```python
import jax
import jax.numpy as jnp
from jax import lax
from jax.sharding import PartitionSpec as P


def collect(values, targets, row_total, first_row=0):
    marks = (
        first_row + jnp.arange(row_total, dtype=jnp.int32)[:, None] == targets[None, :]
    ).astype(jnp.float32)
    flat_rows = values.reshape(values.shape[0], -1)
    summed = jnp.dot(
        marks, flat_rows, precision=lax.Precision.HIGHEST, preferred_element_type=jnp.float32
    )
    return summed.reshape((row_total,) + values.shape[1:])


def tile_product(tile_set, columns, targets, segment_total):
    product = jnp.einsum("tok,trk->tro", tile_set, columns, preferred_element_type=jnp.float32)
    return collect(product, targets, segment_total)


def harm_gather(values, axis):
    count = lax.axis_size("harm")
    own = lax.axis_index("harm")
    parts = [values] + [
        lax.ppermute(values, "harm", [(i, (i + s) % count) for i in range(count)])
        for s in range(1, count)
    ]
    ahead = jnp.stack([parts[(-m) % count] for m in range(count)] * 2, 0)
    ordered = lax.dynamic_slice_in_dim(ahead, (count - own) % count, count, 0)
    ordered = jnp.moveaxis(ordered, 0, axis)
    shape = values.shape[:axis] + (count * values.shape[axis],) + values.shape[axis + 1 :]
    return ordered.reshape(shape)


def on_device(
    right_side,
    border_side,
    precond_tiles,
    tile_out,
    tile_in,
    couple_tiles,
    return_tiles,
    couple_node,
    border_owner,
    border_row,
    border_inverse,
):
    harm_block = precond_tiles.shape[1]
    node_count = right_side.shape[2]
    row_count = border_side.shape[2]
    touch_count = couple_node.shape[0]
    sub_count = lax.axis_size("sub")
    harm_offset = lax.axis_index("harm") * harm_block
    side_nodes = jnp.transpose(right_side, (2, 0, 1))
    border_nodes = jnp.transpose(border_side, (2, 0, 1))
    own_border = lax.dynamic_slice_in_dim(border_nodes, harm_offset, harm_block, 2)
    own_side = lax.dynamic_slice_in_dim(side_nodes, harm_offset, harm_block, 2)
    side_low = side_nodes.astype(jnp.bfloat16)
    first_pass = tile_product(precond_tiles, side_low[tile_in], tile_out, node_count).astype(
        jnp.bfloat16
    )
    first_full = harm_gather(first_pass, 2)
    partials = jnp.einsum(
        "tok,trk->tro", couple_tiles, first_full[couple_node], preferred_element_type=jnp.float32
    )
    owner_list = border_owner[:, 0]
    value_shape = partials.shape[1:]
    capacity = min(touch_count, max(4, 2 * touch_count // sub_count))
    owner_marks = (owner_list[:, None] == jnp.arange(sub_count, dtype=jnp.int32)[None, :]).astype(
        jnp.int32
    )
    earlier = jnp.cumsum(owner_marks, axis=0) - owner_marks
    slot_index = owner_list * capacity + jnp.sum(earlier * owner_marks, axis=1)
    slot_place = jnp.arange(sub_count * capacity, dtype=jnp.int32)[:, None] == slot_index[None, :]
    place_float = slot_place.astype(jnp.float32)
    send_values = jnp.dot(
        place_float,
        partials.reshape(touch_count, -1),
        precision=lax.Precision.HIGHEST,
        preferred_element_type=jnp.float32,
    )
    send_rows = jnp.sum(slot_place.astype(jnp.int32) * border_row[None, :], axis=1)
    row_block = jnp.zeros((sub_count, 128), jnp.float32)
    row_block = row_block.at[:, :capacity].set(
        send_rows.astype(jnp.float32).reshape(sub_count, capacity)
    )
    packet = jnp.concatenate([send_values.reshape(sub_count, -1), row_block], axis=1)
    arrived_packet = lax.all_to_all(packet, "sub", split_axis=0, concat_axis=0, tiled=True)
    value_width = send_values.shape[1]
    arrived = arrived_packet[:, : capacity * value_width].reshape(sub_count * capacity, value_width)
    arrived_rows = arrived_packet[:, capacity * value_width : capacity * value_width + capacity]
    arrived_rows = arrived_rows.astype(jnp.int32).reshape(-1)
    incoming = collect(arrived, arrived_rows, row_count).reshape((row_count,) + value_shape)
    residual_low = (own_border - incoming).astype(jnp.bfloat16)
    residual_full = harm_gather(residual_low, 2)
    solved = jnp.einsum(
        "bok,brk->bro", border_inverse, residual_full, preferred_element_type=jnp.float32
    )
    solved, solved_low = (solved, solved.astype(jnp.bfloat16))
    replies = solved_low[arrived_rows].reshape((sub_count, capacity) + value_shape)
    returned = lax.all_to_all(replies, "sub", split_axis=0, concat_axis=0, tiled=True)
    returned_flat = returned.reshape(sub_count * capacity, -1)
    touch_low = jnp.dot(
        slot_place.astype(jnp.bfloat16).T, returned_flat, preferred_element_type=jnp.float32
    )
    touch_low = touch_low.astype(jnp.bfloat16).reshape((touch_count,) + value_shape)
    touch_full = harm_gather(touch_low, 2)
    correction = tile_product(return_tiles, touch_full, couple_node, node_count)
    update_low = (own_side - correction).astype(jnp.bfloat16)
    update_full = harm_gather(update_low, 2)
    second_pass = tile_product(precond_tiles, update_full[tile_in], tile_out, node_count)
    return (jnp.transpose(second_pass, (1, 2, 0)), jnp.transpose(solved, (1, 2, 0)))


def solution(mesh):
    in_specs = (
        P(None, None, "sub"),
        P(None, None, "sub"),
        P("sub", "harm", None),
        P("sub"),
        P("sub"),
        P("sub", "harm", None),
        P("sub", "harm", None),
        P("sub"),
        P("sub", None),
        P("sub"),
        P("sub", "harm", None),
    )
    out_specs = (P(None, "harm", "sub"), P(None, "harm", "sub"))
    return jax.shard_map(
        on_device, mesh=mesh, in_specs=in_specs, out_specs=out_specs, check_vma=False
    )
```

```python
import jax
import jax.numpy as jnp
from jax import lax
from jax.sharding import PartitionSpec as P


def collect(values, targets, row_total, first_row=0):
    marks = (
        first_row + jnp.arange(row_total, dtype=jnp.int32)[:, None] == targets[None, :]
    ).astype(jnp.float32)
    flat_rows = values.reshape(values.shape[0], -1)
    summed = jnp.dot(
        marks, flat_rows, precision=lax.Precision.HIGHEST, preferred_element_type=jnp.float32
    )
    return summed.reshape((row_total,) + values.shape[1:])


def tile_product(tile_set, columns, targets, segment_total):
    product = jnp.einsum("tok,trk->tro", tile_set, columns, preferred_element_type=jnp.float32)
    return collect(product, targets, segment_total)


def harm_gather(values, axis):
    count = lax.axis_size("harm")
    own = lax.axis_index("harm")
    parts = [values] + [
        lax.ppermute(values, "harm", [(i, (i + s) % count) for i in range(count)])
        for s in range(1, count)
    ]
    blocks = []
    for block in range(count):
        source = (own - block) % count
        chosen = parts[0]
        for s in range(1, count):
            chosen = jnp.where(source == s, parts[s], chosen)
        blocks.append(chosen)
    return jnp.concatenate(blocks, axis)

def on_device(
    right_side,
    border_side,
    precond_tiles,
    tile_out,
    tile_in,
    couple_tiles,
    return_tiles,
    couple_node,
    border_owner,
    border_row,
    border_inverse,
):
    harm_block = precond_tiles.shape[1]
    node_count = right_side.shape[2]
    row_count = border_side.shape[2]
    touch_count = couple_node.shape[0]
    sub_count = lax.axis_size("sub")
    harm_offset = lax.axis_index("harm") * harm_block
    side_nodes = jnp.transpose(right_side, (2, 0, 1))
    border_nodes = jnp.transpose(border_side, (2, 0, 1))
    own_border = lax.dynamic_slice_in_dim(border_nodes, harm_offset, harm_block, 2)
    own_side = lax.dynamic_slice_in_dim(side_nodes, harm_offset, harm_block, 2)
    side_low = side_nodes.astype(jnp.bfloat16)
    halves = [slice(0, side_low.shape[1] // 2), slice(side_low.shape[1] // 2, side_low.shape[1])]
    partial_halves = []
    for half in halves:
        first_pass = tile_product(
            precond_tiles, side_low[:, half][tile_in], tile_out, node_count
        ).astype(jnp.bfloat16)
        first_full = harm_gather(first_pass, 2)
        partial_halves.append(
            jnp.einsum(
                "tok,trk->tro",
                couple_tiles,
                first_full[couple_node],
                preferred_element_type=jnp.float32,
            )
        )
    partials = jnp.concatenate(partial_halves, axis=1)
    owner_list = border_owner[:, 0]
    value_shape = partials.shape[1:]
    capacity = min(touch_count, max(4, 2 * touch_count // sub_count))
    owner_marks = (owner_list[:, None] == jnp.arange(sub_count, dtype=jnp.int32)[None, :]).astype(
        jnp.int32
    )
    earlier = jnp.cumsum(owner_marks, axis=0) - owner_marks
    slot_index = owner_list * capacity + jnp.sum(earlier * owner_marks, axis=1)
    slot_place = jnp.arange(sub_count * capacity, dtype=jnp.int32)[:, None] == slot_index[None, :]
    place_float = slot_place.astype(jnp.float32)
    send_values = jnp.dot(
        place_float,
        partials.reshape(touch_count, -1),
        precision=lax.Precision.HIGHEST,
        preferred_element_type=jnp.float32,
    )
    send_rows = jnp.sum(slot_place.astype(jnp.int32) * border_row[None, :], axis=1)
    row_block = jnp.zeros((sub_count, 128), jnp.float32)
    row_block = row_block.at[:, :capacity].set(
        send_rows.astype(jnp.float32).reshape(sub_count, capacity)
    )
    packet = jnp.concatenate([send_values.reshape(sub_count, -1), row_block], axis=1)
    arrived_packet = lax.all_to_all(packet, "sub", split_axis=0, concat_axis=0, tiled=True)
    value_width = send_values.shape[1]
    arrived = arrived_packet[:, : capacity * value_width].reshape(sub_count * capacity, value_width)
    arrived_rows = arrived_packet[:, capacity * value_width : capacity * value_width + capacity]
    arrived_rows = arrived_rows.astype(jnp.int32).reshape(-1)
    incoming = collect(arrived, arrived_rows, row_count).reshape((row_count,) + value_shape)
    residual_low = (own_border - incoming).astype(jnp.bfloat16)
    residual_full = harm_gather(residual_low, 2)
    solved = jnp.einsum(
        "bok,brk->bro", border_inverse, residual_full, preferred_element_type=jnp.float32
    )
    solved, solved_low = (solved, solved.astype(jnp.bfloat16))
    replies = solved_low[arrived_rows].reshape((sub_count, capacity) + value_shape)
    returned = lax.all_to_all(replies, "sub", split_axis=0, concat_axis=0, tiled=True)
    returned_flat = returned.reshape(sub_count * capacity, -1)
    touch_low = jnp.dot(
        slot_place.astype(jnp.bfloat16).T, returned_flat, preferred_element_type=jnp.float32
    )
    touch_low = touch_low.astype(jnp.bfloat16).reshape((touch_count,) + value_shape)
    second_halves = []
    for half in halves:
        touch_full = harm_gather(touch_low[:, half], 2)
        correction = tile_product(return_tiles, touch_full, couple_node, node_count)
        update_low = (own_side[:, half] - correction).astype(jnp.bfloat16)
        update_full = harm_gather(update_low, 2)
        second_halves.append(
            tile_product(precond_tiles, update_full[tile_in], tile_out, node_count)
        )
    second_pass = jnp.concatenate(second_halves, axis=1)
    return (jnp.transpose(second_pass, (1, 2, 0)), jnp.transpose(solved, (1, 2, 0)))


def solution(mesh):
    in_specs = (
        P(None, None, "sub"),
        P(None, None, "sub"),
        P("sub", "harm", None),
        P("sub"),
        P("sub"),
        P("sub", "harm", None),
        P("sub", "harm", None),
        P("sub"),
        P("sub", None),
        P("sub"),
        P("sub", "harm", None),
    )
    out_specs = (P(None, "harm", "sub"), P(None, "harm", "sub"))
    return jax.shard_map(
        on_device, mesh=mesh, in_specs=in_specs, out_specs=out_specs, check_vma=False
    )
```

```python
import jax
import jax.numpy as jnp
from jax import lax
from jax.sharding import PartitionSpec as P


def collect(values, targets, row_total, first_row=0):
    marks = (
        first_row + jnp.arange(row_total, dtype=jnp.int32)[:, None] == targets[None, :]
    ).astype(jnp.float32)
    flat_rows = values.reshape(values.shape[0], -1)
    summed = jnp.dot(
        marks, flat_rows, precision=lax.Precision.HIGHEST, preferred_element_type=jnp.float32
    )
    return summed.reshape((row_total,) + values.shape[1:])


def tile_product(tile_set, columns, targets, segment_total):
    product = jnp.einsum("tok,trk->tro", tile_set, columns, preferred_element_type=jnp.float32)
    return collect(product, targets, segment_total)


def harm_gather(values, axis):
    count = lax.axis_size("harm")
    own = lax.axis_index("harm")
    parts = [values] + [
        lax.ppermute(values, "harm", [(i, (i + s) % count) for i in range(count)])
        for s in range(1, count)
    ]
    blocks = []
    for block in range(count):
        source = (own - block) % count
        chosen = parts[0]
        for s in range(1, count):
            chosen = jnp.where(source == s, parts[s], chosen)
        blocks.append(chosen)
    return jnp.concatenate(blocks, axis)

def on_device(
    right_side,
    border_side,
    precond_tiles,
    tile_out,
    tile_in,
    couple_tiles,
    return_tiles,
    couple_node,
    border_owner,
    border_row,
    border_inverse,
):
    harm_block = precond_tiles.shape[1]
    node_count = right_side.shape[2]
    row_count = border_side.shape[2]
    touch_count = couple_node.shape[0]
    sub_count = lax.axis_size("sub")
    harm_offset = lax.axis_index("harm") * harm_block
    side_nodes = jnp.transpose(right_side, (2, 0, 1))
    border_nodes = jnp.transpose(border_side, (2, 0, 1))
    own_border = lax.dynamic_slice_in_dim(border_nodes, harm_offset, harm_block, 2)
    own_side = lax.dynamic_slice_in_dim(side_nodes, harm_offset, harm_block, 2)
    side_low = side_nodes.astype(jnp.bfloat16)
    first_pass = tile_product(precond_tiles, side_low[tile_in], tile_out, node_count).astype(
        jnp.bfloat16
    )
    first_full = harm_gather(first_pass, 2)
    partials = jnp.einsum(
        "tok,trk->tro", couple_tiles, first_full[couple_node], preferred_element_type=jnp.float32
    )
    owner_list = border_owner[:, 0]
    value_shape = partials.shape[1:]
    capacity = min(touch_count, max(4, 2 * touch_count // sub_count))
    owner_marks = (owner_list[:, None] == jnp.arange(sub_count, dtype=jnp.int32)[None, :]).astype(
        jnp.int32
    )
    earlier = jnp.cumsum(owner_marks, axis=0) - owner_marks
    slot_index = owner_list * capacity + jnp.sum(earlier * owner_marks, axis=1)
    slot_place = jnp.arange(sub_count * capacity, dtype=jnp.int32)[:, None] == slot_index[None, :]
    place_float = slot_place.astype(jnp.float32)
    send_values = jnp.dot(
        place_float,
        partials.reshape(touch_count, -1),
        precision=lax.Precision.HIGHEST,
        preferred_element_type=jnp.float32,
    )
    send_rows = jnp.sum(slot_place.astype(jnp.int32) * border_row[None, :], axis=1)
    row_block = jnp.zeros((sub_count, 128), jnp.float32)
    row_block = row_block.at[:, :capacity].set(
        send_rows.astype(jnp.float32).reshape(sub_count, capacity)
    )
    packet = jnp.concatenate([send_values.reshape(sub_count, -1), row_block], axis=1)
    arrived_packet = lax.all_to_all(packet, "sub", split_axis=0, concat_axis=0, tiled=True)
    value_width = send_values.shape[1]
    arrived = arrived_packet[:, : capacity * value_width].reshape(sub_count * capacity, value_width)
    arrived_rows = arrived_packet[:, capacity * value_width : capacity * value_width + capacity]
    arrived_rows = arrived_rows.astype(jnp.int32).reshape(-1)
    incoming = collect(arrived, arrived_rows, row_count).reshape((row_count,) + value_shape)
    residual_low = (own_border - incoming).astype(jnp.bfloat16)
    residual_full = harm_gather(residual_low, 2)
    solved = jnp.einsum(
        "bok,brk->bro", border_inverse, residual_full, preferred_element_type=jnp.float32
    )
    solved, solved_low = (solved, solved.astype(jnp.bfloat16))
    replies = solved_low[arrived_rows].reshape((sub_count, capacity) + value_shape)
    returned = lax.all_to_all(replies, "sub", split_axis=0, concat_axis=0, tiled=True)
    returned_flat = returned.reshape(sub_count * capacity, -1)
    touch_low = jnp.dot(
        slot_place.astype(jnp.bfloat16).T, returned_flat, preferred_element_type=jnp.float32
    )
    touch_low = touch_low.astype(jnp.bfloat16).reshape((touch_count,) + value_shape)
    touch_full = harm_gather(touch_low, 2)
    correction = tile_product(return_tiles, touch_full, couple_node, node_count)
    update_low = (own_side - correction).astype(jnp.bfloat16)
    update_full = harm_gather(update_low, 2)
    second_pass = tile_product(precond_tiles, update_full[tile_in], tile_out, node_count)
    return (jnp.transpose(second_pass, (1, 2, 0)), jnp.transpose(solved, (1, 2, 0)))


def solution(mesh):
    in_specs = (
        P(None, None, "sub"),
        P(None, None, "sub"),
        P("sub", "harm", None),
        P("sub"),
        P("sub"),
        P("sub", "harm", None),
        P("sub", "harm", None),
        P("sub"),
        P("sub", None),
        P("sub"),
        P("sub", "harm", None),
    )
    out_specs = (P(None, "harm", "sub"), P(None, "harm", "sub"))
    return jax.shard_map(
        on_device, mesh=mesh, in_specs=in_specs, out_specs=out_specs, check_vma=False
    )
```

```python
import jax
import jax.numpy as jnp
from jax import lax
from jax.sharding import PartitionSpec as P


def collect(values, targets, row_total, first_row=0):
    marks = (
        first_row + jnp.arange(row_total, dtype=jnp.int32)[:, None] == targets[None, :]
    ).astype(jnp.float32)
    flat_rows = values.reshape(values.shape[0], -1)
    summed = jnp.dot(
        marks, flat_rows, precision=lax.Precision.HIGHEST, preferred_element_type=jnp.float32
    )
    return summed.reshape((row_total,) + values.shape[1:])


def tile_product(tile_set, columns, targets, segment_total):
    product = jnp.einsum("tok,trk->tro", tile_set, columns, preferred_element_type=jnp.float32)
    return collect(product, targets, segment_total)


def harm_gather(values, axis):
    count = lax.axis_size("harm")
    own = lax.axis_index("harm")
    parts = [values] + [
        lax.ppermute(values, "harm", [(i, (i + s) % count) for i in range(count)])
        for s in range(1, count)
    ]
    blocks = []
    for block in range(count):
        source = (own - block) % count
        chosen = parts[0]
        for s in range(1, count):
            chosen = jnp.where(source == s, parts[s], chosen)
        blocks.append(chosen)
    return jnp.concatenate(blocks, axis)

def on_device(
    right_side,
    border_side,
    precond_tiles,
    tile_out,
    tile_in,
    couple_tiles,
    return_tiles,
    couple_node,
    border_owner,
    border_row,
    border_inverse,
):
    harm_block = precond_tiles.shape[1]
    node_count = right_side.shape[2]
    row_count = border_side.shape[2]
    touch_count = couple_node.shape[0]
    sub_count = lax.axis_size("sub")
    harm_offset = lax.axis_index("harm") * harm_block
    side_nodes = jnp.transpose(right_side, (2, 0, 1))
    border_nodes = jnp.transpose(border_side, (2, 0, 1))
    own_border = lax.dynamic_slice_in_dim(border_nodes, harm_offset, harm_block, 2)
    own_side = lax.dynamic_slice_in_dim(side_nodes, harm_offset, harm_block, 2)
    side_low = side_nodes.astype(jnp.bfloat16)
    first_pass = tile_product(precond_tiles, side_low[tile_in], tile_out, node_count).astype(
        jnp.bfloat16
    )
    first_full = harm_gather(first_pass, 2)
    partials = jnp.einsum(
        "tok,trk->tro", couple_tiles, first_full[couple_node], preferred_element_type=jnp.float32
    )
    owner_list = border_owner[:, 0]
    value_shape = partials.shape[1:]
    capacity = min(touch_count, max(4, 2 * touch_count // sub_count))
    owner_marks = (owner_list[:, None] == jnp.arange(sub_count, dtype=jnp.int32)[None, :]).astype(
        jnp.int32
    )
    earlier = jnp.cumsum(owner_marks, axis=0) - owner_marks
    slot_index = owner_list * capacity + jnp.sum(earlier * owner_marks, axis=1)
    slot_place = jnp.arange(sub_count * capacity, dtype=jnp.int32)[:, None] == slot_index[None, :]
    place_float = slot_place.astype(jnp.float32)
    send_values = jnp.dot(
        place_float,
        partials.reshape(touch_count, -1),
        precision=lax.Precision.HIGHEST,
        preferred_element_type=jnp.float32,
    )
    send_rows = jnp.sum(slot_place.astype(jnp.int32) * border_row[None, :], axis=1)
    row_block = jnp.zeros((sub_count, 128), jnp.float32)
    row_block = row_block.at[:, :capacity].set(
        send_rows.astype(jnp.float32).reshape(sub_count, capacity)
    )
    packet = jnp.concatenate([send_values.reshape(sub_count, -1), row_block], axis=1)
    arrived_packet = lax.all_to_all(packet, "sub", split_axis=0, concat_axis=0, tiled=True)
    value_width = send_values.shape[1]
    arrived = arrived_packet[:, : capacity * value_width].reshape(sub_count * capacity, value_width)
    arrived_rows = arrived_packet[:, capacity * value_width : capacity * value_width + capacity]
    arrived_rows = arrived_rows.astype(jnp.int32).reshape(-1)
    incoming = collect(arrived, arrived_rows, row_count).reshape((row_count,) + value_shape)
    residual_low = (own_border - incoming).astype(jnp.bfloat16)
    residual_full = harm_gather(residual_low, 2)
    solved = jnp.einsum(
        "bok,brk->bro", border_inverse, residual_full, preferred_element_type=jnp.float32
    )
    solved, solved_low = (solved, solved.astype(jnp.bfloat16))
    reply_marks = arrived_rows[:, None] == jnp.arange(row_count, dtype=jnp.int32)[None, :]
    replies = jnp.dot(
        reply_marks.astype(jnp.bfloat16),
        solved_low.reshape(row_count, -1),
        preferred_element_type=jnp.float32,
    ).astype(jnp.bfloat16)
    returned = lax.all_to_all(
        replies.reshape(sub_count, -1), "sub", split_axis=0, concat_axis=0, tiled=True
    )
    returned_flat = returned.reshape(sub_count * capacity, -1)
    touch_low = jnp.dot(
        slot_place.astype(jnp.bfloat16).T, returned_flat, preferred_element_type=jnp.float32
    )
    touch_low = touch_low.astype(jnp.bfloat16).reshape((touch_count,) + value_shape)
    touch_full = harm_gather(touch_low, 2)
    correction = tile_product(return_tiles, touch_full, couple_node, node_count)
    update_low = (own_side - correction).astype(jnp.bfloat16)
    update_full = harm_gather(update_low, 2)
    second_pass = tile_product(precond_tiles, update_full[tile_in], tile_out, node_count)
    return (jnp.transpose(second_pass, (1, 2, 0)), jnp.transpose(solved, (1, 2, 0)))


def solution(mesh):
    in_specs = (
        P(None, None, "sub"),
        P(None, None, "sub"),
        P("sub", "harm", None),
        P("sub"),
        P("sub"),
        P("sub", "harm", None),
        P("sub", "harm", None),
        P("sub"),
        P("sub", None),
        P("sub"),
        P("sub", "harm", None),
    )
    out_specs = (P(None, "harm", "sub"), P(None, "harm", "sub"))
    return jax.shard_map(
        on_device, mesh=mesh, in_specs=in_specs, out_specs=out_specs, check_vma=False
    )
```

```python
import jax
import jax.numpy as jnp
from jax import lax
from jax.sharding import PartitionSpec as P


def collect(values, targets, row_total, first_row=0):
    marks = (
        first_row + jnp.arange(row_total, dtype=jnp.int32)[:, None] == targets[None, :]
    ).astype(jnp.float32)
    return jnp.tensordot(marks, values, axes=1, precision=lax.Precision.HIGHEST)


def tile_product(tile_set, columns, targets, segment_total):
    product = jnp.einsum("tok,trk->tro", tile_set, columns, preferred_element_type=jnp.float32)
    return collect(product, targets, segment_total)


def harm_gather(values, axis):
    count = lax.axis_size("harm")
    own = lax.axis_index("harm")
    parts = [values] + [
        lax.ppermute(values, "harm", [(i, (i + s) % count) for i in range(count)])
        for s in range(1, count)
    ]
    blocks = []
    for block in range(count):
        source = (own - block) % count
        chosen = parts[0]
        for s in range(1, count):
            chosen = jnp.where(source == s, parts[s], chosen)
        blocks.append(chosen)
    return jnp.concatenate(blocks, axis)

def on_device(
    right_side,
    border_side,
    precond_tiles,
    tile_out,
    tile_in,
    couple_tiles,
    return_tiles,
    couple_node,
    border_owner,
    border_row,
    border_inverse,
):
    harm_block = precond_tiles.shape[1]
    node_count = right_side.shape[2]
    row_count = border_side.shape[2]
    touch_count = couple_node.shape[0]
    sub_count = lax.axis_size("sub")
    harm_offset = lax.axis_index("harm") * harm_block
    side_nodes = jnp.transpose(right_side, (2, 0, 1))
    border_nodes = jnp.transpose(border_side, (2, 0, 1))
    own_border = lax.dynamic_slice_in_dim(border_nodes, harm_offset, harm_block, 2)
    own_side = lax.dynamic_slice_in_dim(side_nodes, harm_offset, harm_block, 2)
    side_low = side_nodes.astype(jnp.bfloat16)
    first_pass = tile_product(precond_tiles, side_low[tile_in], tile_out, node_count).astype(
        jnp.bfloat16
    )
    first_full = harm_gather(first_pass, 2)
    partials = jnp.einsum(
        "tok,trk->tro", couple_tiles, first_full[couple_node], preferred_element_type=jnp.float32
    )
    owner_list = border_owner[:, 0]
    value_shape = partials.shape[1:]
    capacity = min(touch_count, max(4, 2 * touch_count // sub_count))
    owner_marks = (owner_list[:, None] == jnp.arange(sub_count, dtype=jnp.int32)[None, :]).astype(
        jnp.int32
    )
    earlier = jnp.cumsum(owner_marks, axis=0) - owner_marks
    slot_index = owner_list * capacity + jnp.sum(earlier * owner_marks, axis=1)
    slot_place = jnp.arange(sub_count * capacity, dtype=jnp.int32)[:, None] == slot_index[None, :]
    place_float = slot_place.astype(jnp.float32)
    send_values = jnp.dot(
        place_float,
        partials.reshape(touch_count, -1),
        precision=lax.Precision.HIGHEST,
        preferred_element_type=jnp.float32,
    )
    send_rows = jnp.sum(slot_place.astype(jnp.int32) * border_row[None, :], axis=1)
    row_block = jnp.zeros((sub_count, 128), jnp.float32)
    row_block = row_block.at[:, :capacity].set(
        send_rows.astype(jnp.float32).reshape(sub_count, capacity)
    )
    packet = jnp.concatenate([send_values.reshape(sub_count, -1), row_block], axis=1)
    arrived_packet = lax.all_to_all(packet, "sub", split_axis=0, concat_axis=0, tiled=True)
    value_width = send_values.shape[1]
    arrived = arrived_packet[:, : capacity * value_width].reshape(sub_count * capacity, value_width)
    arrived_rows = arrived_packet[:, capacity * value_width : capacity * value_width + capacity]
    arrived_rows = arrived_rows.astype(jnp.int32).reshape(-1)
    incoming = collect(arrived, arrived_rows, row_count).reshape((row_count,) + value_shape)
    residual_low = (own_border - incoming).astype(jnp.bfloat16)
    residual_full = harm_gather(residual_low, 2)
    solved = jnp.einsum(
        "bok,brk->bro", border_inverse, residual_full, preferred_element_type=jnp.float32
    )
    solved, solved_low = (solved, solved.astype(jnp.bfloat16))
    replies = solved_low[arrived_rows].reshape((sub_count, capacity) + value_shape)
    returned = lax.all_to_all(replies, "sub", split_axis=0, concat_axis=0, tiled=True)
    returned_flat = returned.reshape(sub_count * capacity, -1)
    touch_low = jnp.dot(
        slot_place.astype(jnp.bfloat16).T, returned_flat, preferred_element_type=jnp.float32
    )
    touch_low = touch_low.astype(jnp.bfloat16).reshape((touch_count,) + value_shape)
    touch_full = harm_gather(touch_low, 2)
    correction = tile_product(return_tiles, touch_full, couple_node, node_count)
    update_low = (own_side - correction).astype(jnp.bfloat16)
    update_full = harm_gather(update_low, 2)
    second_pass = tile_product(precond_tiles, update_full[tile_in], tile_out, node_count)
    return (jnp.transpose(second_pass, (1, 2, 0)), jnp.transpose(solved, (1, 2, 0)))


def solution(mesh):
    in_specs = (
        P(None, None, "sub"),
        P(None, None, "sub"),
        P("sub", "harm", None),
        P("sub"),
        P("sub"),
        P("sub", "harm", None),
        P("sub", "harm", None),
        P("sub"),
        P("sub", None),
        P("sub"),
        P("sub", "harm", None),
    )
    out_specs = (P(None, "harm", "sub"), P(None, "harm", "sub"))
    return jax.shard_map(
        on_device, mesh=mesh, in_specs=in_specs, out_specs=out_specs, check_vma=False
    )
```

```python
import jax
import jax.numpy as jnp
from jax import lax
from jax.sharding import PartitionSpec as P


def collect(values, targets, row_total, first_row=0):
    marks = (
        first_row + jnp.arange(row_total, dtype=jnp.int32)[:, None] == targets[None, :]
    ).astype(jnp.float32)
    flat_rows = values.reshape(values.shape[0], -1)
    summed = jnp.dot(
        marks, flat_rows, precision=lax.Precision.HIGHEST, preferred_element_type=jnp.float32
    )
    return summed.reshape((row_total,) + values.shape[1:])


def tile_product(tile_set, columns, targets, segment_total):
    product = jnp.einsum("tok,trk->tro", tile_set, columns, preferred_element_type=jnp.float32)
    return collect(product, targets, segment_total)


def pick_rows(table, rows):
    marks = (rows[:, None] == jnp.arange(table.shape[0], dtype=jnp.int32)[None, :]).astype(
        table.dtype
    )
    picked = jnp.einsum("tn,nrk->trk", marks, table, preferred_element_type=jnp.float32)
    return picked.astype(table.dtype)


def harm_gather(values, axis):
    count = lax.axis_size("harm")
    own = lax.axis_index("harm")
    parts = [values] + [
        lax.ppermute(values, "harm", [(i, (i + s) % count) for i in range(count)])
        for s in range(1, count)
    ]
    blocks = []
    for block in range(count):
        source = (own - block) % count
        chosen = parts[0]
        for s in range(1, count):
            chosen = jnp.where(source == s, parts[s], chosen)
        blocks.append(chosen)
    return jnp.concatenate(blocks, axis)

def on_device(
    right_side,
    border_side,
    precond_tiles,
    tile_out,
    tile_in,
    couple_tiles,
    return_tiles,
    couple_node,
    border_owner,
    border_row,
    border_inverse,
):
    harm_block = precond_tiles.shape[1]
    node_count = right_side.shape[2]
    row_count = border_side.shape[2]
    touch_count = couple_node.shape[0]
    sub_count = lax.axis_size("sub")
    harm_offset = lax.axis_index("harm") * harm_block
    side_nodes = jnp.transpose(right_side, (2, 0, 1))
    border_nodes = jnp.transpose(border_side, (2, 0, 1))
    own_border = lax.dynamic_slice_in_dim(border_nodes, harm_offset, harm_block, 2)
    own_side = lax.dynamic_slice_in_dim(side_nodes, harm_offset, harm_block, 2)
    side_low = side_nodes.astype(jnp.bfloat16)
    first_pass = tile_product(precond_tiles, pick_rows(side_low, tile_in), tile_out, node_count).astype(
        jnp.bfloat16
    )
    first_full = harm_gather(first_pass, 2)
    partials = jnp.einsum(
        "tok,trk->tro", couple_tiles, pick_rows(first_full, couple_node), preferred_element_type=jnp.float32
    )
    owner_list = border_owner[:, 0]
    value_shape = partials.shape[1:]
    capacity = min(touch_count, max(4, 2 * touch_count // sub_count))
    owner_marks = (owner_list[:, None] == jnp.arange(sub_count, dtype=jnp.int32)[None, :]).astype(
        jnp.int32
    )
    earlier = jnp.cumsum(owner_marks, axis=0) - owner_marks
    slot_index = owner_list * capacity + jnp.sum(earlier * owner_marks, axis=1)
    slot_place = jnp.arange(sub_count * capacity, dtype=jnp.int32)[:, None] == slot_index[None, :]
    place_float = slot_place.astype(jnp.float32)
    send_values = jnp.dot(
        place_float,
        partials.reshape(touch_count, -1),
        precision=lax.Precision.HIGHEST,
        preferred_element_type=jnp.float32,
    )
    send_rows = jnp.sum(slot_place.astype(jnp.int32) * border_row[None, :], axis=1)
    row_block = jnp.zeros((sub_count, 128), jnp.float32)
    row_block = row_block.at[:, :capacity].set(
        send_rows.astype(jnp.float32).reshape(sub_count, capacity)
    )
    packet = jnp.concatenate([send_values.reshape(sub_count, -1), row_block], axis=1)
    arrived_packet = lax.all_to_all(packet, "sub", split_axis=0, concat_axis=0, tiled=True)
    value_width = send_values.shape[1]
    arrived = arrived_packet[:, : capacity * value_width].reshape(sub_count * capacity, value_width)
    arrived_rows = arrived_packet[:, capacity * value_width : capacity * value_width + capacity]
    arrived_rows = arrived_rows.astype(jnp.int32).reshape(-1)
    incoming = collect(arrived, arrived_rows, row_count).reshape((row_count,) + value_shape)
    residual_low = (own_border - incoming).astype(jnp.bfloat16)
    residual_full = harm_gather(residual_low, 2)
    solved = jnp.einsum(
        "bok,brk->bro", border_inverse, residual_full, preferred_element_type=jnp.float32
    )
    solved, solved_low = (solved, solved.astype(jnp.bfloat16))
    replies = solved_low[arrived_rows].reshape((sub_count, capacity) + value_shape)
    returned = lax.all_to_all(replies, "sub", split_axis=0, concat_axis=0, tiled=True)
    returned_flat = returned.reshape(sub_count * capacity, -1)
    touch_low = jnp.dot(
        slot_place.astype(jnp.bfloat16).T, returned_flat, preferred_element_type=jnp.float32
    )
    touch_low = touch_low.astype(jnp.bfloat16).reshape((touch_count,) + value_shape)
    touch_full = harm_gather(touch_low, 2)
    correction = tile_product(return_tiles, touch_full, couple_node, node_count)
    update_low = (own_side - correction).astype(jnp.bfloat16)
    update_full = harm_gather(update_low, 2)
    second_pass = tile_product(precond_tiles, pick_rows(update_full, tile_in), tile_out, node_count)
    return (jnp.transpose(second_pass, (1, 2, 0)), jnp.transpose(solved, (1, 2, 0)))


def solution(mesh):
    in_specs = (
        P(None, None, "sub"),
        P(None, None, "sub"),
        P("sub", "harm", None),
        P("sub"),
        P("sub"),
        P("sub", "harm", None),
        P("sub", "harm", None),
        P("sub"),
        P("sub", None),
        P("sub"),
        P("sub", "harm", None),
    )
    out_specs = (P(None, "harm", "sub"), P(None, "harm", "sub"))
    return jax.shard_map(
        on_device, mesh=mesh, in_specs=in_specs, out_specs=out_specs, check_vma=False
    )
```

```python
import jax
import jax.numpy as jnp
from jax import lax
from jax.sharding import PartitionSpec as P


def collect(values, targets, row_total, first_row=0):
    marks = (
        first_row + jnp.arange(row_total, dtype=jnp.int32)[:, None] == targets[None, :]
    ).astype(jnp.float32)
    flat_rows = values.reshape(values.shape[0], -1)
    summed = jnp.dot(
        marks, flat_rows, precision=lax.Precision.HIGHEST, preferred_element_type=jnp.float32
    )
    return summed.reshape((row_total,) + values.shape[1:])


def tile_product(tile_set, columns, targets, segment_total):
    product = jnp.einsum("tok,trk->tro", tile_set, columns, preferred_element_type=jnp.float32)
    return collect(product, targets, segment_total)


def pick_rows(table, rows):
    marks = (rows[:, None] == jnp.arange(table.shape[0], dtype=jnp.int32)[None, :]).astype(
        table.dtype
    )
    picked = jnp.einsum("tn,nrk->trk", marks, table, preferred_element_type=jnp.float32)
    return picked.astype(table.dtype)


def harm_gather(values, axis):
    count = lax.axis_size("harm")
    own = lax.axis_index("harm")
    parts = [values] + [
        lax.ppermute(values, "harm", [(i, (i + s) % count) for i in range(count)])
        for s in range(1, count)
    ]
    blocks = []
    for block in range(count):
        source = (own - block) % count
        chosen = parts[0]
        for s in range(1, count):
            chosen = jnp.where(source == s, parts[s], chosen)
        blocks.append(chosen)
    return jnp.concatenate(blocks, axis)

def on_device(
    right_side,
    border_side,
    precond_tiles,
    tile_out,
    tile_in,
    couple_tiles,
    return_tiles,
    couple_node,
    border_owner,
    border_row,
    border_inverse,
):
    harm_block = precond_tiles.shape[1]
    node_count = right_side.shape[2]
    row_count = border_side.shape[2]
    touch_count = couple_node.shape[0]
    sub_count = lax.axis_size("sub")
    harm_offset = lax.axis_index("harm") * harm_block
    side_nodes = jnp.transpose(right_side, (2, 0, 1))
    border_nodes = jnp.transpose(border_side, (2, 0, 1))
    own_border = lax.dynamic_slice_in_dim(border_nodes, harm_offset, harm_block, 2)
    own_side = lax.dynamic_slice_in_dim(side_nodes, harm_offset, harm_block, 2)
    side_low = side_nodes.astype(jnp.bfloat16)
    first_pass = tile_product(precond_tiles, pick_rows(side_low, tile_in), tile_out, node_count).astype(
        jnp.bfloat16
    )
    first_full = harm_gather(first_pass, 2)
    partials = jnp.einsum(
        "tok,trk->tro", couple_tiles, pick_rows(first_full, couple_node), preferred_element_type=jnp.float32
    )
    owner_list = border_owner[:, 0]
    value_shape = partials.shape[1:]
    capacity = min(touch_count, max(4, 2 * touch_count // sub_count))
    owner_marks = (owner_list[:, None] == jnp.arange(sub_count, dtype=jnp.int32)[None, :]).astype(
        jnp.int32
    )
    earlier = jnp.cumsum(owner_marks, axis=0) - owner_marks
    slot_index = owner_list * capacity + jnp.sum(earlier * owner_marks, axis=1)
    slot_place = jnp.arange(sub_count * capacity, dtype=jnp.int32)[:, None] == slot_index[None, :]
    place_float = slot_place.astype(jnp.float32)
    send_values = jnp.dot(
        place_float,
        partials.reshape(touch_count, -1),
        precision=lax.Precision.HIGHEST,
        preferred_element_type=jnp.float32,
    )
    send_rows = jnp.sum(slot_place.astype(jnp.int32) * border_row[None, :], axis=1)
    row_block = jnp.zeros((sub_count, 128), jnp.float32)
    row_block = row_block.at[:, :capacity].set(
        send_rows.astype(jnp.float32).reshape(sub_count, capacity)
    )
    packet = jnp.concatenate([send_values.reshape(sub_count, -1), row_block], axis=1)
    arrived_packet = lax.all_to_all(packet, "sub", split_axis=0, concat_axis=0, tiled=True)
    value_width = send_values.shape[1]
    arrived = arrived_packet[:, : capacity * value_width].reshape(sub_count * capacity, value_width)
    arrived_rows = arrived_packet[:, capacity * value_width : capacity * value_width + capacity]
    arrived_rows = arrived_rows.astype(jnp.int32).reshape(-1)
    incoming = collect(arrived, arrived_rows, row_count).reshape((row_count,) + value_shape)
    residual_low = (own_border - incoming).astype(jnp.bfloat16)
    residual_full = harm_gather(residual_low, 2)
    solved = jnp.einsum(
        "bok,brk->bro", border_inverse, residual_full, preferred_element_type=jnp.float32
    )
    solved, solved_low = (solved, solved.astype(jnp.bfloat16))
    replies = pick_rows(solved_low, arrived_rows).reshape((sub_count, capacity) + value_shape)
    returned = lax.all_to_all(replies, "sub", split_axis=0, concat_axis=0, tiled=True)
    returned_flat = returned.reshape(sub_count * capacity, -1)
    touch_low = jnp.dot(
        slot_place.astype(jnp.bfloat16).T, returned_flat, preferred_element_type=jnp.float32
    )
    touch_low = touch_low.astype(jnp.bfloat16).reshape((touch_count,) + value_shape)
    touch_full = harm_gather(touch_low, 2)
    correction = tile_product(return_tiles, touch_full, couple_node, node_count)
    update_low = (own_side - correction).astype(jnp.bfloat16)
    update_full = harm_gather(update_low, 2)
    second_pass = tile_product(precond_tiles, pick_rows(update_full, tile_in), tile_out, node_count)
    return (jnp.transpose(second_pass, (1, 2, 0)), jnp.transpose(solved, (1, 2, 0)))


def solution(mesh):
    in_specs = (
        P(None, None, "sub"),
        P(None, None, "sub"),
        P("sub", "harm", None),
        P("sub"),
        P("sub"),
        P("sub", "harm", None),
        P("sub", "harm", None),
        P("sub"),
        P("sub", None),
        P("sub"),
        P("sub", "harm", None),
    )
    out_specs = (P(None, "harm", "sub"), P(None, "harm", "sub"))
    return jax.shard_map(
        on_device, mesh=mesh, in_specs=in_specs, out_specs=out_specs, check_vma=False
    )
```

```python
import jax
import jax.numpy as jnp
from jax import lax
from jax.sharding import PartitionSpec as P


def collect(values, targets, row_total, first_row=0):
    marks = (
        first_row + jnp.arange(row_total, dtype=jnp.int32)[:, None] == targets[None, :]
    ).astype(jnp.float32)
    flat_rows = values.reshape(values.shape[0], -1)
    summed = jnp.dot(
        marks, flat_rows, precision=lax.Precision.HIGHEST, preferred_element_type=jnp.float32
    )
    return summed.reshape((row_total,) + values.shape[1:])


def tile_product(tile_set, columns, targets, segment_total):
    product = jnp.einsum("tok,trk->rot", tile_set, columns, preferred_element_type=jnp.float32)
    marks = (
        jnp.arange(segment_total, dtype=jnp.int32)[:, None] == targets[None, :]
    ).astype(jnp.float32)
    return jnp.einsum("nt,rot->nro", marks, product, precision=lax.Precision.HIGHEST)

def pick_rows(table, rows):
    marks = (rows[:, None] == jnp.arange(table.shape[0], dtype=jnp.int32)[None, :]).astype(
        table.dtype
    )
    picked = jnp.einsum("tn,nrk->trk", marks, table, preferred_element_type=jnp.float32)
    return picked.astype(table.dtype)


def harm_gather(values, axis):
    count = lax.axis_size("harm")
    own = lax.axis_index("harm")
    parts = [values] + [
        lax.ppermute(values, "harm", [(i, (i + s) % count) for i in range(count)])
        for s in range(1, count)
    ]
    blocks = []
    for block in range(count):
        source = (own - block) % count
        chosen = parts[0]
        for s in range(1, count):
            chosen = jnp.where(source == s, parts[s], chosen)
        blocks.append(chosen)
    return jnp.concatenate(blocks, axis)

def on_device(
    right_side,
    border_side,
    precond_tiles,
    tile_out,
    tile_in,
    couple_tiles,
    return_tiles,
    couple_node,
    border_owner,
    border_row,
    border_inverse,
):
    harm_block = precond_tiles.shape[1]
    node_count = right_side.shape[2]
    row_count = border_side.shape[2]
    touch_count = couple_node.shape[0]
    sub_count = lax.axis_size("sub")
    harm_offset = lax.axis_index("harm") * harm_block
    side_nodes = jnp.transpose(right_side, (2, 0, 1))
    border_nodes = jnp.transpose(border_side, (2, 0, 1))
    own_border = lax.dynamic_slice_in_dim(border_nodes, harm_offset, harm_block, 2)
    own_side = lax.dynamic_slice_in_dim(side_nodes, harm_offset, harm_block, 2)
    side_low = side_nodes.astype(jnp.bfloat16)
    first_pass = tile_product(precond_tiles, pick_rows(side_low, tile_in), tile_out, node_count).astype(
        jnp.bfloat16
    )
    first_full = harm_gather(first_pass, 2)
    partials = jnp.einsum(
        "tok,trk->tro", couple_tiles, pick_rows(first_full, couple_node), preferred_element_type=jnp.float32
    )
    owner_list = border_owner[:, 0]
    value_shape = partials.shape[1:]
    capacity = min(touch_count, max(4, 2 * touch_count // sub_count))
    owner_marks = (owner_list[:, None] == jnp.arange(sub_count, dtype=jnp.int32)[None, :]).astype(
        jnp.int32
    )
    earlier = jnp.cumsum(owner_marks, axis=0) - owner_marks
    slot_index = owner_list * capacity + jnp.sum(earlier * owner_marks, axis=1)
    slot_place = jnp.arange(sub_count * capacity, dtype=jnp.int32)[:, None] == slot_index[None, :]
    place_float = slot_place.astype(jnp.float32)
    send_values = jnp.dot(
        place_float,
        partials.reshape(touch_count, -1),
        precision=lax.Precision.HIGHEST,
        preferred_element_type=jnp.float32,
    )
    send_rows = jnp.sum(slot_place.astype(jnp.int32) * border_row[None, :], axis=1)
    row_block = jnp.zeros((sub_count, 128), jnp.float32)
    row_block = row_block.at[:, :capacity].set(
        send_rows.astype(jnp.float32).reshape(sub_count, capacity)
    )
    packet = jnp.concatenate([send_values.reshape(sub_count, -1), row_block], axis=1)
    arrived_packet = lax.all_to_all(packet, "sub", split_axis=0, concat_axis=0, tiled=True)
    value_width = send_values.shape[1]
    arrived = arrived_packet[:, : capacity * value_width].reshape(sub_count * capacity, value_width)
    arrived_rows = arrived_packet[:, capacity * value_width : capacity * value_width + capacity]
    arrived_rows = arrived_rows.astype(jnp.int32).reshape(-1)
    incoming = collect(arrived, arrived_rows, row_count).reshape((row_count,) + value_shape)
    residual_low = (own_border - incoming).astype(jnp.bfloat16)
    residual_full = harm_gather(residual_low, 2)
    solved = jnp.einsum(
        "bok,brk->bro", border_inverse, residual_full, preferred_element_type=jnp.float32
    )
    solved, solved_low = (solved, solved.astype(jnp.bfloat16))
    replies = solved_low[arrived_rows].reshape((sub_count, capacity) + value_shape)
    returned = lax.all_to_all(replies, "sub", split_axis=0, concat_axis=0, tiled=True)
    returned_flat = returned.reshape(sub_count * capacity, -1)
    touch_low = jnp.dot(
        slot_place.astype(jnp.bfloat16).T, returned_flat, preferred_element_type=jnp.float32
    )
    touch_low = touch_low.astype(jnp.bfloat16).reshape((touch_count,) + value_shape)
    touch_full = harm_gather(touch_low, 2)
    correction = tile_product(return_tiles, touch_full, couple_node, node_count)
    update_low = (own_side - correction).astype(jnp.bfloat16)
    update_full = harm_gather(update_low, 2)
    second_pass = tile_product(precond_tiles, pick_rows(update_full, tile_in), tile_out, node_count)
    return (jnp.transpose(second_pass, (1, 2, 0)), jnp.transpose(solved, (1, 2, 0)))


def solution(mesh):
    in_specs = (
        P(None, None, "sub"),
        P(None, None, "sub"),
        P("sub", "harm", None),
        P("sub"),
        P("sub"),
        P("sub", "harm", None),
        P("sub", "harm", None),
        P("sub"),
        P("sub", None),
        P("sub"),
        P("sub", "harm", None),
    )
    out_specs = (P(None, "harm", "sub"), P(None, "harm", "sub"))
    return jax.shard_map(
        on_device, mesh=mesh, in_specs=in_specs, out_specs=out_specs, check_vma=False
    )
```

```python
import jax
import jax.numpy as jnp
from jax import lax
from jax.sharding import PartitionSpec as P


def collect(values, targets, row_total, first_row=0):
    marks = (
        first_row + jnp.arange(row_total, dtype=jnp.int32)[:, None] == targets[None, :]
    ).astype(jnp.float32)
    flat_rows = values.reshape(values.shape[0], -1)
    summed = jnp.dot(
        marks, flat_rows, precision=lax.Precision.HIGHEST, preferred_element_type=jnp.float32
    )
    return summed.reshape((row_total,) + values.shape[1:])


def tile_product(tile_set, columns, targets, segment_total):
    product = jnp.einsum("tok,trk->tro", tile_set, columns, preferred_element_type=jnp.float32)
    return collect(product, targets, segment_total)


def pick_rows(table, rows):
    marks = (rows[:, None] == jnp.arange(table.shape[0], dtype=jnp.int32)[None, :]).astype(
        table.dtype
    )
    picked = jnp.einsum("tn,nrk->trk", marks, table, preferred_element_type=jnp.float32)
    return picked.astype(table.dtype)


def harm_gather(values, axis):
    count = lax.axis_size("harm")
    own = lax.axis_index("harm")
    parts = [values] + [
        lax.ppermute(values, "harm", [(i, (i + s) % count) for i in range(count)])
        for s in range(1, count)
    ]
    blocks = []
    for block in range(count):
        source = (own - block) % count
        chosen = parts[0]
        for s in range(1, count):
            chosen = jnp.where(source == s, parts[s], chosen)
        blocks.append(chosen)
    return jnp.concatenate(blocks, axis)

def on_device(
    right_side,
    border_side,
    precond_tiles,
    tile_out,
    tile_in,
    couple_tiles,
    return_tiles,
    couple_node,
    border_owner,
    border_row,
    border_inverse,
):
    harm_block = precond_tiles.shape[1]
    node_count = right_side.shape[2]
    row_count = border_side.shape[2]
    touch_count = couple_node.shape[0]
    sub_count = lax.axis_size("sub")
    harm_offset = lax.axis_index("harm") * harm_block
    side_nodes = jnp.transpose(right_side, (2, 0, 1))
    border_nodes = jnp.transpose(border_side, (2, 0, 1))
    own_border = lax.dynamic_slice_in_dim(border_nodes, harm_offset, harm_block, 2)
    own_side = lax.dynamic_slice_in_dim(side_nodes, harm_offset, harm_block, 2)
    side_low = side_nodes.astype(jnp.bfloat16)
    first_pass = tile_product(precond_tiles, pick_rows(side_low, tile_in), tile_out, node_count).astype(
        jnp.bfloat16
    )
    first_full = harm_gather(first_pass, 2)
    partials = jnp.einsum(
        "tok,trk->tro", couple_tiles, pick_rows(first_full, couple_node), preferred_element_type=jnp.float32
    )
    owner_list = border_owner[:, 0]
    value_shape = partials.shape[1:]
    capacity = min(touch_count, max(4, 2 * touch_count // sub_count))
    owner_marks = (owner_list[:, None] == jnp.arange(sub_count, dtype=jnp.int32)[None, :]).astype(
        jnp.int32
    )
    earlier = jnp.cumsum(owner_marks, axis=0) - owner_marks
    slot_index = owner_list * capacity + jnp.sum(earlier * owner_marks, axis=1)
    slot_place = jnp.arange(sub_count * capacity, dtype=jnp.int32)[:, None] == slot_index[None, :]
    place_float = slot_place.astype(jnp.float32)
    send_values = jnp.dot(
        place_float,
        partials.reshape(touch_count, -1),
        precision=lax.Precision.HIGHEST,
        preferred_element_type=jnp.float32,
    )
    send_rows = jnp.sum(slot_place.astype(jnp.int32) * border_row[None, :], axis=1)
    row_block = jnp.zeros((sub_count, 128), jnp.float32)
    row_block = row_block.at[:, :capacity].set(
        send_rows.astype(jnp.float32).reshape(sub_count, capacity)
    )
    packet = jnp.concatenate([send_values.reshape(sub_count, -1), row_block], axis=1)
    arrived_packet = lax.all_to_all(packet, "sub", split_axis=0, concat_axis=0, tiled=True)
    value_width = send_values.shape[1]
    arrived = arrived_packet[:, : capacity * value_width].reshape(sub_count * capacity, value_width)
    arrived_rows = arrived_packet[:, capacity * value_width : capacity * value_width + capacity]
    arrived_rows = arrived_rows.astype(jnp.int32).reshape(-1)
    incoming = collect(arrived, arrived_rows, row_count).reshape((row_count,) + value_shape)
    residual_low = (own_border - incoming).astype(jnp.bfloat16)
    residual_full = harm_gather(residual_low, 2)
    solved = jnp.einsum(
        "bok,brk->bro", border_inverse, residual_full, preferred_element_type=jnp.float32
    )
    solved, solved_low = (solved, solved.astype(jnp.bfloat16))
    replies = solved_low[arrived_rows].reshape((sub_count, capacity) + value_shape)
    returned = lax.all_to_all(replies, "sub", split_axis=0, concat_axis=0, tiled=True)
    returned_flat = returned.reshape(sub_count * capacity, -1)
    touch_low = jnp.dot(
        slot_place.astype(jnp.bfloat16).T, returned_flat, preferred_element_type=jnp.float32
    )
    touch_low = touch_low.astype(jnp.bfloat16).reshape((touch_count,) + value_shape)
    touch_full = pick_rows(harm_gather(touch_low, 2), jnp.arange(touch_count, dtype=jnp.int32))
    correction = tile_product(return_tiles, touch_full, couple_node, node_count)
    update_low = (own_side - correction).astype(jnp.bfloat16)
    update_full = harm_gather(update_low, 2)
    second_pass = tile_product(precond_tiles, pick_rows(update_full, tile_in), tile_out, node_count)
    return (jnp.transpose(second_pass, (1, 2, 0)), jnp.transpose(solved, (1, 2, 0)))


def solution(mesh):
    in_specs = (
        P(None, None, "sub"),
        P(None, None, "sub"),
        P("sub", "harm", None),
        P("sub"),
        P("sub"),
        P("sub", "harm", None),
        P("sub", "harm", None),
        P("sub"),
        P("sub", None),
        P("sub"),
        P("sub", "harm", None),
    )
    out_specs = (P(None, "harm", "sub"), P(None, "harm", "sub"))
    return jax.shard_map(
        on_device, mesh=mesh, in_specs=in_specs, out_specs=out_specs, check_vma=False
    )
```

```python
import jax
import jax.numpy as jnp
from jax import lax
from jax.sharding import PartitionSpec as P


def collect(values, targets, row_total, first_row=0):
    marks = (
        first_row + jnp.arange(row_total, dtype=jnp.int32)[:, None] == targets[None, :]
    ).astype(jnp.float32)
    flat_rows = values.reshape(values.shape[0], -1)
    summed = jnp.dot(
        marks, flat_rows, precision=lax.Precision.HIGHEST, preferred_element_type=jnp.float32
    )
    return summed.reshape((row_total,) + values.shape[1:])


def tile_product(tile_set, columns, targets, segment_total):
    product = jnp.einsum("tok,trk->tro", tile_set, columns, preferred_element_type=jnp.float32)
    return collect(product, targets, segment_total)


def pick_rows(table, rows):
    marks = (rows[:, None] == jnp.arange(table.shape[0], dtype=jnp.int32)[None, :]).astype(
        table.dtype
    )
    picked = jnp.einsum("tn,nrk->trk", marks, table, preferred_element_type=jnp.float32)
    return picked.astype(table.dtype)


def harm_gather(values, axis):
    count = lax.axis_size("harm")
    own = lax.axis_index("harm")
    parts = [values] + [
        lax.ppermute(values, "harm", [(i, (i + s) % count) for i in range(count)])
        for s in range(1, count)
    ]
    blocks = []
    for block in range(count):
        source = (own - block) % count
        chosen = parts[0]
        for s in range(1, count):
            chosen = jnp.where(source == s, parts[s], chosen)
        blocks.append(chosen)
    return jnp.concatenate(blocks, axis)

def on_device(
    right_side,
    border_side,
    precond_tiles,
    tile_out,
    tile_in,
    couple_tiles,
    return_tiles,
    couple_node,
    border_owner,
    border_row,
    border_inverse,
):
    harm_block = precond_tiles.shape[1]
    node_count = right_side.shape[2]
    row_count = border_side.shape[2]
    touch_count = couple_node.shape[0]
    sub_count = lax.axis_size("sub")
    harm_offset = lax.axis_index("harm") * harm_block
    side_nodes = jnp.transpose(right_side, (2, 0, 1))
    border_nodes = jnp.transpose(border_side, (2, 0, 1))
    own_border = lax.dynamic_slice_in_dim(border_nodes, harm_offset, harm_block, 2)
    own_side = lax.dynamic_slice_in_dim(side_nodes, harm_offset, harm_block, 2)
    side_low = side_nodes.astype(jnp.bfloat16)
    first_pass = tile_product(precond_tiles, pick_rows(side_low, tile_in), tile_out, node_count).astype(
        jnp.bfloat16
    )
    first_full = harm_gather(first_pass, 2)
    partials = jnp.einsum(
        "tok,trk->tro", couple_tiles, pick_rows(first_full, couple_node), preferred_element_type=jnp.float32
    )
    owner_list = border_owner[:, 0]
    value_shape = partials.shape[1:]
    capacity = min(touch_count, max(4, 2 * touch_count // sub_count))
    owner_marks = (owner_list[:, None] == jnp.arange(sub_count, dtype=jnp.int32)[None, :]).astype(
        jnp.int32
    )
    earlier = jnp.cumsum(owner_marks, axis=0) - owner_marks
    slot_index = owner_list * capacity + jnp.sum(earlier * owner_marks, axis=1)
    slot_place = jnp.arange(sub_count * capacity, dtype=jnp.int32)[:, None] == slot_index[None, :]
    place_float = slot_place.astype(jnp.float32)
    send_values = jnp.dot(
        place_float,
        partials.reshape(touch_count, -1),
        precision=lax.Precision.HIGHEST,
        preferred_element_type=jnp.float32,
    )
    send_rows = jnp.sum(slot_place.astype(jnp.int32) * border_row[None, :], axis=1)
    row_block = jnp.zeros((sub_count, 128), jnp.float32)
    row_block = row_block.at[:, :capacity].set(
        send_rows.astype(jnp.float32).reshape(sub_count, capacity)
    )
    packet = jnp.concatenate([send_values.reshape(sub_count, -1), row_block], axis=1)
    arrived_packet = lax.all_to_all(packet, "sub", split_axis=0, concat_axis=0, tiled=True)
    value_width = send_values.shape[1]
    arrived = arrived_packet[:, : capacity * value_width].reshape(sub_count * capacity, value_width)
    arrived_rows = arrived_packet[:, capacity * value_width : capacity * value_width + capacity]
    arrived_rows = arrived_rows.astype(jnp.int32).reshape(-1)
    incoming = collect(arrived, arrived_rows, row_count).reshape((row_count,) + value_shape)
    residual_low = (own_border - incoming).astype(jnp.bfloat16)
    residual_full = pick_rows(harm_gather(residual_low, 2), jnp.arange(row_count, dtype=jnp.int32))
    solved = jnp.einsum(
        "bok,brk->bro", border_inverse, residual_full, preferred_element_type=jnp.float32
    )
    solved, solved_low = (solved, solved.astype(jnp.bfloat16))
    replies = solved_low[arrived_rows].reshape((sub_count, capacity) + value_shape)
    returned = lax.all_to_all(replies, "sub", split_axis=0, concat_axis=0, tiled=True)
    returned_flat = returned.reshape(sub_count * capacity, -1)
    touch_low = jnp.dot(
        slot_place.astype(jnp.bfloat16).T, returned_flat, preferred_element_type=jnp.float32
    )
    touch_low = touch_low.astype(jnp.bfloat16).reshape((touch_count,) + value_shape)
    touch_full = pick_rows(harm_gather(touch_low, 2), jnp.arange(touch_count, dtype=jnp.int32))
    correction = tile_product(return_tiles, touch_full, couple_node, node_count)
    update_low = (own_side - correction).astype(jnp.bfloat16)
    update_full = harm_gather(update_low, 2)
    second_pass = tile_product(precond_tiles, pick_rows(update_full, tile_in), tile_out, node_count)
    return (jnp.transpose(second_pass, (1, 2, 0)), jnp.transpose(solved, (1, 2, 0)))


def solution(mesh):
    in_specs = (
        P(None, None, "sub"),
        P(None, None, "sub"),
        P("sub", "harm", None),
        P("sub"),
        P("sub"),
        P("sub", "harm", None),
        P("sub", "harm", None),
        P("sub"),
        P("sub", None),
        P("sub"),
        P("sub", "harm", None),
    )
    out_specs = (P(None, "harm", "sub"), P(None, "harm", "sub"))
    return jax.shard_map(
        on_device, mesh=mesh, in_specs=in_specs, out_specs=out_specs, check_vma=False
    )
```

```python
import jax
import jax.numpy as jnp
from jax import lax
from jax.sharding import PartitionSpec as P


def collect(values, targets, row_total, first_row=0):
    marks = (
        first_row + jnp.arange(row_total, dtype=jnp.int32)[:, None] == targets[None, :]
    ).astype(jnp.float32)
    flat_rows = values.reshape(values.shape[0], -1)
    summed = jnp.dot(
        marks, flat_rows, precision=lax.Precision.HIGHEST, preferred_element_type=jnp.float32
    )
    return summed.reshape((row_total,) + values.shape[1:])


def tile_product(tile_set, columns, targets, segment_total):
    product = jnp.einsum("tok,trk->rot", tile_set, columns, preferred_element_type=jnp.float32)
    marks = (
        jnp.arange(segment_total, dtype=jnp.int32)[:, None] == targets[None, :]
    ).astype(jnp.float32)
    return jnp.einsum("nt,rot->nro", marks, product, precision=lax.Precision.HIGHEST)

def pick_rows(table, rows):
    marks = (rows[:, None] == jnp.arange(table.shape[0], dtype=jnp.int32)[None, :]).astype(
        table.dtype
    )
    picked = jnp.einsum("tn,nrk->trk", marks, table, preferred_element_type=jnp.float32)
    return picked.astype(table.dtype)


def harm_gather(values, axis):
    count = lax.axis_size("harm")
    own = lax.axis_index("harm")
    parts = [values] + [
        lax.ppermute(values, "harm", [(i, (i + s) % count) for i in range(count)])
        for s in range(1, count)
    ]
    blocks = []
    for block in range(count):
        source = (own - block) % count
        chosen = parts[0]
        for s in range(1, count):
            chosen = jnp.where(source == s, parts[s], chosen)
        blocks.append(chosen)
    return jnp.concatenate(blocks, axis)

def on_device(
    right_side,
    border_side,
    precond_tiles,
    tile_out,
    tile_in,
    couple_tiles,
    return_tiles,
    couple_node,
    border_owner,
    border_row,
    border_inverse,
):
    harm_block = precond_tiles.shape[1]
    node_count = right_side.shape[2]
    row_count = border_side.shape[2]
    touch_count = couple_node.shape[0]
    sub_count = lax.axis_size("sub")
    harm_offset = lax.axis_index("harm") * harm_block
    side_nodes = jnp.transpose(right_side, (2, 0, 1))
    border_nodes = jnp.transpose(border_side, (2, 0, 1))
    own_border = lax.dynamic_slice_in_dim(border_nodes, harm_offset, harm_block, 2)
    own_side = lax.dynamic_slice_in_dim(side_nodes, harm_offset, harm_block, 2)
    side_low = side_nodes.astype(jnp.bfloat16)
    first_pass = tile_product(precond_tiles, pick_rows(side_low, tile_in), tile_out, node_count).astype(
        jnp.bfloat16
    )
    first_full = harm_gather(first_pass, 2)
    partials = jnp.einsum(
        "tok,trk->tro", couple_tiles, pick_rows(first_full, couple_node), preferred_element_type=jnp.float32
    )
    owner_list = border_owner[:, 0]
    value_shape = partials.shape[1:]
    capacity = min(touch_count, max(4, 2 * touch_count // sub_count))
    owner_marks = (owner_list[:, None] == jnp.arange(sub_count, dtype=jnp.int32)[None, :]).astype(
        jnp.int32
    )
    earlier = jnp.cumsum(owner_marks, axis=0) - owner_marks
    slot_index = owner_list * capacity + jnp.sum(earlier * owner_marks, axis=1)
    slot_place = jnp.arange(sub_count * capacity, dtype=jnp.int32)[:, None] == slot_index[None, :]
    place_float = slot_place.astype(jnp.float32)
    send_values = jnp.dot(
        place_float,
        partials.reshape(touch_count, -1),
        precision=lax.Precision.HIGHEST,
        preferred_element_type=jnp.float32,
    )
    send_rows = jnp.sum(slot_place.astype(jnp.int32) * border_row[None, :], axis=1)
    row_block = jnp.zeros((sub_count, 128), jnp.float32)
    row_block = row_block.at[:, :capacity].set(
        send_rows.astype(jnp.float32).reshape(sub_count, capacity)
    )
    packet = jnp.concatenate([send_values.reshape(sub_count, -1), row_block], axis=1)
    arrived_packet = lax.all_to_all(packet, "sub", split_axis=0, concat_axis=0, tiled=True)
    value_width = send_values.shape[1]
    arrived = arrived_packet[:, : capacity * value_width].reshape(sub_count * capacity, value_width)
    arrived_rows = arrived_packet[:, capacity * value_width : capacity * value_width + capacity]
    arrived_rows = arrived_rows.astype(jnp.int32).reshape(-1)
    incoming = collect(arrived, arrived_rows, row_count).reshape((row_count,) + value_shape)
    residual_low = (own_border - incoming).astype(jnp.bfloat16)
    residual_full = pick_rows(harm_gather(residual_low, 2), jnp.arange(row_count, dtype=jnp.int32))
    solved = jnp.einsum(
        "bok,brk->bro", border_inverse, residual_full, preferred_element_type=jnp.float32
    )
    solved, solved_low = (solved, solved.astype(jnp.bfloat16))
    replies = solved_low[arrived_rows].reshape((sub_count, capacity) + value_shape)
    returned = lax.all_to_all(replies, "sub", split_axis=0, concat_axis=0, tiled=True)
    returned_flat = returned.reshape(sub_count * capacity, -1)
    touch_low = jnp.dot(
        slot_place.astype(jnp.bfloat16).T, returned_flat, preferred_element_type=jnp.float32
    )
    touch_low = touch_low.astype(jnp.bfloat16).reshape((touch_count,) + value_shape)
    touch_full = pick_rows(harm_gather(touch_low, 2), jnp.arange(touch_count, dtype=jnp.int32))
    correction = tile_product(return_tiles, touch_full, couple_node, node_count)
    update_low = (own_side - correction).astype(jnp.bfloat16)
    update_full = harm_gather(update_low, 2)
    second_pass = tile_product(precond_tiles, pick_rows(update_full, tile_in), tile_out, node_count)
    return (jnp.transpose(second_pass, (1, 2, 0)), jnp.transpose(solved, (1, 2, 0)))


def solution(mesh):
    in_specs = (
        P(None, None, "sub"),
        P(None, None, "sub"),
        P("sub", "harm", None),
        P("sub"),
        P("sub"),
        P("sub", "harm", None),
        P("sub", "harm", None),
        P("sub"),
        P("sub", None),
        P("sub"),
        P("sub", "harm", None),
    )
    out_specs = (P(None, "harm", "sub"), P(None, "harm", "sub"))
    return jax.shard_map(
        on_device, mesh=mesh, in_specs=in_specs, out_specs=out_specs, check_vma=False
    )
```

```python
import jax
import jax.numpy as jnp
from jax import lax
from jax.sharding import PartitionSpec as P


def collect(values, targets, row_total, first_row=0):
    marks = (
        first_row + jnp.arange(row_total, dtype=jnp.int32)[:, None] == targets[None, :]
    ).astype(jnp.float32)
    flat_rows = values.reshape(values.shape[0], -1)
    summed = jnp.dot(
        marks, flat_rows, precision=lax.Precision.HIGHEST, preferred_element_type=jnp.float32
    )
    return summed.reshape((row_total,) + values.shape[1:])


def tile_product(tile_set, columns, targets, segment_total):
    product = jnp.einsum("tok,trk->tro", tile_set, columns, preferred_element_type=jnp.float32)
    return collect(product, targets, segment_total)


def pick_rows(table, rows):
    marks = (rows[:, None] == jnp.arange(table.shape[0], dtype=jnp.int32)[None, :]).astype(
        table.dtype
    )
    picked = jnp.einsum("tn,nrk->trk", marks, table, preferred_element_type=jnp.float32)
    return picked.astype(table.dtype)


def harm_gather(values, axis):
    count = lax.axis_size("harm")
    own = lax.axis_index("harm")
    parts = [values] + [
        lax.ppermute(values, "harm", [(i, (i + s) % count) for i in range(count)])
        for s in range(1, count)
    ]
    blocks = []
    for block in range(count):
        source = (own - block) % count
        chosen = parts[0]
        for s in range(1, count):
            chosen = jnp.where(source == s, parts[s], chosen)
        blocks.append(chosen)
    return jnp.concatenate(blocks, axis)

def on_device(
    right_side,
    border_side,
    precond_tiles,
    tile_out,
    tile_in,
    couple_tiles,
    return_tiles,
    couple_node,
    border_owner,
    border_row,
    border_inverse,
):
    harm_block = precond_tiles.shape[1]
    node_count = right_side.shape[2]
    row_count = border_side.shape[2]
    touch_count = couple_node.shape[0]
    sub_count = lax.axis_size("sub")
    harm_offset = lax.axis_index("harm") * harm_block
    side_nodes = jnp.transpose(right_side, (2, 0, 1))
    border_nodes = jnp.transpose(border_side, (2, 0, 1))
    own_border = lax.dynamic_slice_in_dim(border_nodes, harm_offset, harm_block, 2)
    own_side = lax.dynamic_slice_in_dim(side_nodes, harm_offset, harm_block, 2)
    side_low = side_nodes.astype(jnp.bfloat16)
    first_pass = tile_product(precond_tiles, pick_rows(side_low, tile_in), tile_out, node_count).astype(
        jnp.bfloat16
    )
    first_full = harm_gather(first_pass, 2)
    partials = jnp.einsum(
        "tok,trk->rot", couple_tiles, pick_rows(first_full, couple_node), preferred_element_type=jnp.float32
    )
    owner_list = border_owner[:, 0]
    value_shape = (partials.shape[0], partials.shape[1])
    capacity = min(touch_count, max(4, 2 * touch_count // sub_count))
    owner_marks = (owner_list[:, None] == jnp.arange(sub_count, dtype=jnp.int32)[None, :]).astype(
        jnp.int32
    )
    earlier = jnp.cumsum(owner_marks, axis=0) - owner_marks
    slot_index = owner_list * capacity + jnp.sum(earlier * owner_marks, axis=1)
    slot_place = jnp.arange(sub_count * capacity, dtype=jnp.int32)[:, None] == slot_index[None, :]
    place_float = slot_place.astype(jnp.float32)
    send_values = jnp.einsum(
        "st,rot->sro", place_float, partials, precision=lax.Precision.HIGHEST
    ).reshape(place_float.shape[0], -1)
    send_rows = jnp.sum(slot_place.astype(jnp.int32) * border_row[None, :], axis=1)
    row_block = jnp.zeros((sub_count, 128), jnp.float32)
    row_block = row_block.at[:, :capacity].set(
        send_rows.astype(jnp.float32).reshape(sub_count, capacity)
    )
    packet = jnp.concatenate([send_values.reshape(sub_count, -1), row_block], axis=1)
    arrived_packet = lax.all_to_all(packet, "sub", split_axis=0, concat_axis=0, tiled=True)
    value_width = send_values.shape[1]
    arrived = arrived_packet[:, : capacity * value_width].reshape(sub_count * capacity, value_width)
    arrived_rows = arrived_packet[:, capacity * value_width : capacity * value_width + capacity]
    arrived_rows = arrived_rows.astype(jnp.int32).reshape(-1)
    incoming = collect(arrived, arrived_rows, row_count).reshape((row_count,) + value_shape)
    residual_low = (own_border - incoming).astype(jnp.bfloat16)
    residual_full = pick_rows(harm_gather(residual_low, 2), jnp.arange(row_count, dtype=jnp.int32))
    solved = jnp.einsum(
        "bok,brk->bro", border_inverse, residual_full, preferred_element_type=jnp.float32
    )
    solved, solved_low = (solved, solved.astype(jnp.bfloat16))
    replies = solved_low[arrived_rows].reshape((sub_count, capacity) + value_shape)
    returned = lax.all_to_all(replies, "sub", split_axis=0, concat_axis=0, tiled=True)
    returned_flat = returned.reshape(sub_count * capacity, -1)
    touch_low = jnp.dot(
        slot_place.astype(jnp.bfloat16).T, returned_flat, preferred_element_type=jnp.float32
    )
    touch_low = touch_low.astype(jnp.bfloat16).reshape((touch_count,) + value_shape)
    touch_full = pick_rows(harm_gather(touch_low, 2), jnp.arange(touch_count, dtype=jnp.int32))
    correction = tile_product(return_tiles, touch_full, couple_node, node_count)
    update_low = (own_side - correction).astype(jnp.bfloat16)
    update_full = harm_gather(update_low, 2)
    second_pass = tile_product(precond_tiles, pick_rows(update_full, tile_in), tile_out, node_count)
    return (jnp.transpose(second_pass, (1, 2, 0)), jnp.transpose(solved, (1, 2, 0)))


def solution(mesh):
    in_specs = (
        P(None, None, "sub"),
        P(None, None, "sub"),
        P("sub", "harm", None),
        P("sub"),
        P("sub"),
        P("sub", "harm", None),
        P("sub", "harm", None),
        P("sub"),
        P("sub", None),
        P("sub"),
        P("sub", "harm", None),
    )
    out_specs = (P(None, "harm", "sub"), P(None, "harm", "sub"))
    return jax.shard_map(
        on_device, mesh=mesh, in_specs=in_specs, out_specs=out_specs, check_vma=False
    )
```
